256 devices in a mesh: fsdp: 16 (over z_hi, x), tensor: 16 (over z_lo, y, core).
Axes of the slice: x: 4, y: 4, z: 8 (z_hi: 4, z_lo: 2; z = z_hi * 2 + z_lo), core: 2. Of those that a mesh axis runs over, the one named last changes fastest.
Arguments:
- tokens: bfloat16 [8192, 3072], P('fsdp'), may hold values from -6 to 6
- weights: bfloat16 [3072, 4, 4096], P('fsdp', None, 'tensor'), may hold values from -0.109375 to 0.109375
- direction: bfloat16 [3072, 4, 4096], P('fsdp', None, 'tensor'), may hold values from -0.109375 to 0.109375
- precision: float32 [3072], replicated, may hold values from 0.25 to 4
Outputs:
- ggn: float32 [3072, 4, 4096], P('fsdp', None, 'tensor')
The draws below stay inside these ranges and needn't reach their ends.
All inputs are finite; a program needn't handle non-finite values.
Results may differ from the reference program's by a relative error of at most 0.015.
Values may be sent and summed in bfloat16 or wider, within the bound.
No kernel may reach another device: no remote copies, remote signals or barrier semaphores. Data moves between devices by JAX's collectives and lax.ppermute only.
A program may use at most 128 MiB of HBM per device.

```python
import math
import jax
import jax.numpy as jnp
from jax import lax

D = 3072
HEAD = 128
PATCHES = 256
HD = 4096
TOKENS = 8192
N_TENSOR = 16


def raised(result, stream_key, source, target, blocks, factor):
    def block_of(axis_at):
        return (jnp.arange(result.shape[axis_at]) // (result.shape[axis_at] // blocks)).reshape((-1,) + (1,) * (result.ndim - 1 - axis_at))

    one_side = jax.random.permutation(stream_key, blocks)[block_of(target)]
    other_side = (block_of(target) + blocks // 2) % blocks
    return jnp.where((block_of(source) == one_side) | (block_of(source) == other_side), factor * result, result)


def level_of(stream_key, shape, shards, smallest, top_value):
    def one(dim, shards_of):
        draws = jax.random.uniform(jax.random.fold_in(jax.random.fold_in(stream_key, 6), dim), (shards_of,), jnp.float32, smallest / len(shards), top_value / len(shards))
        return jnp.repeat(jnp.exp(draws), shape[dim] // shards_of).reshape((-1,) + (1,) * (len(shape) - dim - 1))

    level = one(*shards[0])
    for cut in shards[1:]:
        level = level * one(*cut)
    return level


def scatter_about(stream_key, extent, deviation, most, shards=(), kind=jnp.bfloat16):
    array = jax.random.normal(stream_key, extent, jnp.float32) * deviation
    if len(shards) > 0:
        array = level_of(stream_key, extent, shards, -0.22, 0.18) * array
    return jnp.clip(array, min=-most, max=most).astype(kind)


def bell_draw_with(rng, dims, deviation, limit, cuts, heavy, held_as=jnp.bfloat16):
    values = deviation * jax.random.normal(rng, dims, jnp.float32)
    if cuts:
        values = values * level_of(rng, dims, cuts, -0.22, 0.18)
    return jnp.clip(raised(values, jax.random.fold_in(rng, 3), *heavy), -limit, limit).astype(held_as)


def setup_inputs(seed: int = 0) -> dict:
    streams_of = jax.random.split(jax.random.key(seed), 5)
    return {
        "tokens": bell_draw_with(streams_of[0], (TOKENS, D), 1.0, 6.0, ((0, 16),), (0, 1, 16, 2.0)),
        "weights": scatter_about(streams_of[1], (D, 4, HD), D ** -0.5, 0.109375, ((0, 16), (2, 16))),
        "direction": scatter_about(streams_of[2], (D, 4, HD), D ** -0.5, 0.109375, ((0, 16), (2, 16))),
        "precision": jnp.clip(jnp.exp(jax.random.uniform(streams_of[3], (D,), jnp.float32, math.log(0.25), math.log(4.0))), 0.25, 4.0),
    }


def layer_norm(rows):
    mean_row = lax.optimization_barrier(jnp.mean(rows, -1, keepdims=True))
    centred = rows - mean_row
    spread = lax.optimization_barrier(jnp.mean(centred * centred, -1, keepdims=True))
    return centred * lax.rsqrt(spread + 1e-06)

def attend(queries, key_rows, value_rows):
    query_norm = layer_norm(queries)
    key_norm = layer_norm(key_rows)
    score_scale = queries.shape[-1] ** (-0.5)
    scores = jnp.einsum('bqhe,bkhe->bhqk', query_norm, key_norm, precision=lax.Precision.HIGHEST) * score_scale
    exponent = jnp.exp(scores)
    attn_weights = exponent / lax.optimization_barrier(jnp.sum(exponent, -1, keepdims=True))
    return jnp.einsum('bhqk,bkhe->bqhe', attn_weights, value_rows, precision=lax.Precision.HIGHEST)

def reference(tokens, weights, direction, precision):
    model_width = tokens.shape[1]
    total_rows = tokens.shape[0]
    head_cols = weights.shape[2]
    normed = layer_norm(tokens.astype(jnp.float32)).astype(jnp.bfloat16)
    in_weights = weights[:, 0:3, :].reshape(model_width, 3 * head_cols)
    in_direction = direction[:, 0:3, :].reshape(model_width, 3 * head_cols)
    projected = jnp.dot(normed, in_weights, preferred_element_type=jnp.float32).astype(jnp.bfloat16)
    tangent_in = jnp.dot(normed, in_direction, preferred_element_type=jnp.float32).astype(jnp.bfloat16)

    def to_heads(block):
        return block.astype(jnp.float32).reshape(total_rows // PATCHES, PATCHES, 3, head_cols // HEAD, HEAD)
    primal = to_heads(projected)
    tangent_heads = to_heads(tangent_in)
    primal_args = (primal[:, :, 0], primal[:, :, 1], primal[:, :, 2])
    tangent_args = (tangent_heads[:, :, 0], tangent_heads[:, :, 1], tangent_heads[:, :, 2])
    mixed, mixed_dot = jax.jvp(attend, primal_args, tangent_args)
    mixed_rows = mixed.reshape(total_rows, head_cols).astype(jnp.bfloat16)
    tangent_out = mixed_dot.reshape(total_rows, head_cols).astype(jnp.bfloat16)
    out_weights = weights[:, 3, :]
    out_direction = direction[:, 3, :]
    group_cols = head_cols // N_TENSOR
    output_dot = jnp.zeros((total_rows, model_width), jnp.float32)
    for group_index in range(N_TENSOR):
        first_col = group_index * group_cols
        last_col = first_col + group_cols
        partial_sum = jnp.dot(tangent_out[:, first_col:last_col], out_weights[:, first_col:last_col].T, preferred_element_type=jnp.float32)
        partial_sum = partial_sum + jnp.dot(mixed_rows[:, first_col:last_col], out_direction[:, first_col:last_col].T, preferred_element_type=jnp.float32)
        rounded = lax.optimization_barrier(partial_sum.astype(jnp.bfloat16))
        output_dot = output_dot + rounded.astype(jnp.float32)
    cotangent = (precision * output_dot).astype(jnp.bfloat16)
    out_grad = jnp.dot(cotangent.T, mixed_rows, preferred_element_type=jnp.float32)
    back_rows = jnp.dot(cotangent, out_weights, preferred_element_type=jnp.float32)
    back_rows = back_rows.reshape(total_rows // PATCHES, PATCHES, head_cols // HEAD, HEAD)
    primal_out, pullback = jax.vjp(attend, *primal_args)
    gradients = pullback(back_rows)
    stacked = jnp.stack(gradients, axis=2).reshape(total_rows, 3 * head_cols).astype(jnp.bfloat16)
    in_grad = jnp.dot(normed.T, stacked, preferred_element_type=jnp.float32).reshape(model_width, 3, head_cols)
    return jnp.concatenate([in_grad, out_grad[:, None, :]], axis=1)
```

```python
import jax
import jax.numpy as jnp
from jax import lax
from jax.sharding import PartitionSpec as P

HEAD = 128
PATCHES = 256


def layer_norm(rows):
    mean_row = jnp.mean(rows, -1, keepdims=True)
    centred = rows - mean_row
    spread = jnp.mean(centred * centred, -1, keepdims=True)
    return centred * lax.rsqrt(spread + 1e-06)


def attend(queries, key_rows, value_rows):
    query_norm = layer_norm(queries)
    key_norm = layer_norm(key_rows)
    score_scale = queries.shape[-1] ** (-0.5)
    scores = (
        jnp.einsum("bqhe,bkhe->bhqk", query_norm, key_norm, precision=lax.Precision.HIGHEST)
        * score_scale
    )
    exponent = jnp.exp(scores)
    attn_weights = exponent / jnp.sum(exponent, -1, keepdims=True)
    return jnp.einsum("bhqk,bkhe->bqhe", attn_weights, value_rows, precision=lax.Precision.HIGHEST)


def cross_rows(left, right):
    return lax.dot_general(
        left, right, (((1,), (1,)), ((), ())), preferred_element_type=jnp.float32
    )


def over_tokens(left, right):
    return lax.dot_general(
        left, right, (((0,), (0,)), ((), ())), preferred_element_type=jnp.float32
    )


def body(tokens, weights, direction, precision):
    model_width = tokens.shape[1]
    local_rows = tokens.shape[0]
    head_cols = weights.shape[2]
    normed = layer_norm(tokens.astype(jnp.float32)).astype(jnp.bfloat16)
    both = lax.all_gather(jnp.concatenate([weights, direction], 1), "fsdp", axis=0, tiled=True)
    full_weights = both[:, 0:4]
    full_direction = both[:, 4:8]
    in_weights = full_weights[:, 0:3, :].reshape(model_width, 3 * head_cols)
    in_direction = full_direction[:, 0:3, :].reshape(model_width, 3 * head_cols)
    projected = jnp.dot(normed, in_weights, preferred_element_type=jnp.float32).astype(jnp.bfloat16)
    tangent_in = jnp.dot(normed, in_direction, preferred_element_type=jnp.float32).astype(
        jnp.bfloat16
    )

    def to_heads(block):
        return block.astype(jnp.float32).reshape(
            local_rows // PATCHES, PATCHES, 3, head_cols // HEAD, HEAD
        )

    primal = to_heads(projected)
    tangent_heads = to_heads(tangent_in)
    primal_args = (primal[:, :, 0], primal[:, :, 1], primal[:, :, 2])
    tangent_args = (tangent_heads[:, :, 0], tangent_heads[:, :, 1], tangent_heads[:, :, 2])
    mixed, mixed_dot = jax.jvp(attend, primal_args, tangent_args)
    mixed_rows = mixed.reshape(local_rows, head_cols).astype(jnp.bfloat16)
    tangent_out = mixed_dot.reshape(local_rows, head_cols).astype(jnp.bfloat16)
    out_weights = full_weights[:, 3, :]
    out_direction = full_direction[:, 3, :]
    partial_sum = cross_rows(tangent_out, out_weights) + cross_rows(mixed_rows, out_direction)
    n_tensor = lax.axis_size("tensor")
    chunk = model_width // n_tensor
    arrived = lax.all_to_all(
        partial_sum.astype(jnp.bfloat16).reshape(local_rows, n_tensor, chunk), "tensor", 1, 1
    )
    output_dot = jnp.sum(arrived.astype(jnp.float32), 1)
    own_precision = lax.dynamic_slice_in_dim(precision, lax.axis_index("tensor") * chunk, chunk)
    cotangent_part = (own_precision * output_dot).astype(jnp.bfloat16)
    spread = jnp.broadcast_to(cotangent_part[None], (n_tensor, local_rows, chunk))
    cotangent = jnp.moveaxis(lax.all_to_all(spread, "tensor", 0, 0), 0, 1).reshape(
        local_rows, model_width
    )
    share_rows = model_width // lax.axis_size("fsdp")
    back_rows = jnp.dot(cotangent, out_weights, preferred_element_type=jnp.float32)
    back_rows = back_rows.reshape(local_rows // PATCHES, PATCHES, head_cols // HEAD, HEAD)
    primal_out, pullback = jax.vjp(attend, *primal_args)
    gradients = pullback(back_rows)
    stacked = jnp.stack(gradients, axis=2).reshape(local_rows, 3 * head_cols).astype(jnp.bfloat16)
    return lax.psum_scatter(
        jnp.concatenate(
            [
                over_tokens(normed, stacked).reshape(
                    lax.axis_size("fsdp") * share_rows, 3, head_cols
                ),
                over_tokens(cotangent, mixed_rows)[:, None, :],
            ],
            axis=1,
        ).astype(jnp.bfloat16),
        "fsdp",
        scatter_dimension=0,
        tiled=True,
    ).astype(jnp.float32)


def solution(mesh):
    return jax.shard_map(
        body,
        mesh=mesh,
        in_specs=(P("fsdp", None), P("fsdp", None, "tensor"), P("fsdp", None, "tensor"), P()),
        out_specs=P("fsdp", None, "tensor"),
        check_vma=False,
    )
```

```python
import jax
import jax.numpy as jnp
from jax import lax
from jax.sharding import PartitionSpec as P

HEAD = 128
PATCHES = 256


def layer_norm(rows):
    mean_row = jnp.mean(rows, -1, keepdims=True)
    centred = rows - mean_row
    spread = jnp.mean(centred * centred, -1, keepdims=True)
    return centred * lax.rsqrt(spread + 1e-06)


def attend(queries, key_rows, value_rows):
    query_norm = layer_norm(queries)
    key_norm = layer_norm(key_rows)
    score_scale = queries.shape[-1] ** (-0.5)
    scores = (
        jnp.einsum("bqhe,bkhe->bhqk", query_norm, key_norm, precision=lax.Precision.HIGHEST)
        * score_scale
    )
    exponent = jnp.exp(scores)
    attn_weights = exponent / jnp.sum(exponent, -1, keepdims=True)
    return jnp.einsum("bhqk,bkhe->bqhe", attn_weights, value_rows, precision=lax.Precision.HIGHEST)


def cross_rows(left, right):
    return lax.dot_general(
        left, right, (((1,), (1,)), ((), ())), preferred_element_type=jnp.float32
    )


def over_tokens(left, right):
    return lax.dot_general(
        left, right, (((0,), (0,)), ((), ())), preferred_element_type=jnp.float32
    )


def body(tokens, weights, direction, precision):
    model_width = tokens.shape[1]
    local_rows = tokens.shape[0]
    share_rows = weights.shape[0]
    head_cols = weights.shape[2]
    normed = layer_norm(tokens.astype(jnp.float32)).astype(jnp.bfloat16)
    local = jnp.concatenate(
        [weights[:, 0:3], direction[:, 0:3], weights[:, 3:4], direction[:, 3:4]], 1
    ).reshape(share_rows, 8 * head_cols)
    gathered = lax.all_gather(local.T, "fsdp", axis=1, tiled=True)
    in_both = gathered[: 6 * head_cols]
    out_both = gathered[6 * head_cols :]
    both_in = cross_rows(normed, in_both).astype(jnp.bfloat16)
    projected = both_in[:, : 3 * head_cols]
    tangent_in = both_in[:, 3 * head_cols :]

    def to_heads(block):
        return block.astype(jnp.float32).reshape(
            local_rows // PATCHES, PATCHES, 3, head_cols // HEAD, HEAD
        )

    primal = to_heads(projected)
    tangent_heads = to_heads(tangent_in)
    primal_args = (primal[:, :, 0], primal[:, :, 1], primal[:, :, 2])
    tangent_args = (tangent_heads[:, :, 0], tangent_heads[:, :, 1], tangent_heads[:, :, 2])
    mixed, mixed_dot = jax.jvp(attend, primal_args, tangent_args)
    mixed_rows = mixed.reshape(local_rows, head_cols).astype(jnp.bfloat16)
    tangent_out = mixed_dot.reshape(local_rows, head_cols).astype(jnp.bfloat16)
    partial_sum = lax.dot_general(
        jnp.concatenate([tangent_out, mixed_rows], 1),
        out_both,
        (((1,), (0,)), ((), ())),
        preferred_element_type=jnp.float32,
    )
    n_tensor = lax.axis_size("tensor")
    chunk = model_width // n_tensor
    arrived = lax.all_to_all(
        partial_sum.astype(jnp.bfloat16).reshape(local_rows, n_tensor, chunk), "tensor", 1, 1
    )
    output_dot = jnp.sum(arrived.astype(jnp.float32), 1)
    own_precision = lax.dynamic_slice_in_dim(precision, lax.axis_index("tensor") * chunk, chunk)
    cotangent_part = (own_precision * output_dot).astype(jnp.bfloat16)
    spread = jnp.broadcast_to(cotangent_part[None], (n_tensor, local_rows, chunk))
    cotangent = jnp.moveaxis(lax.all_to_all(spread, "tensor", 0, 0), 0, 1).reshape(
        local_rows, model_width
    )
    back_rows = cross_rows(cotangent, out_both[:head_cols])
    back_rows = back_rows.reshape(local_rows // PATCHES, PATCHES, head_cols // HEAD, HEAD)
    primal_out, pullback = jax.vjp(attend, *primal_args)
    gradients = pullback(back_rows)
    stacked = jnp.stack(gradients, axis=2).reshape(local_rows, 3 * head_cols).astype(jnp.bfloat16)
    return lax.psum_scatter(
        jnp.concatenate(
            [
                over_tokens(normed, stacked).reshape(model_width, 3, head_cols),
                over_tokens(cotangent, mixed_rows)[:, None, :],
            ],
            axis=1,
        ).astype(jnp.bfloat16),
        "fsdp",
        scatter_dimension=0,
        tiled=True,
    ).astype(jnp.float32)


def solution(mesh):
    return jax.shard_map(
        body,
        mesh=mesh,
        in_specs=(P("fsdp", None), P("fsdp", None, "tensor"), P("fsdp", None, "tensor"), P()),
        out_specs=P("fsdp", None, "tensor"),
        check_vma=False,
    )
```

```python
import jax
import jax.numpy as jnp
from jax import lax
from jax.sharding import Mesh, PartitionSpec as P

FSDP = ("z_hi", "x")
TENSOR = ("z_lo", "y", "core")

HEAD = 128
PATCHES = 256


def layer_norm(rows):
    mean_row = jnp.mean(rows, -1, keepdims=True)
    centred = rows - mean_row
    spread = jnp.mean(centred * centred, -1, keepdims=True)
    return centred * lax.rsqrt(spread + 1e-06)


def attend(queries, key_rows, value_rows):
    query_norm = layer_norm(queries)
    key_norm = layer_norm(key_rows)
    score_scale = queries.shape[-1] ** (-0.5)
    scores = (
        jnp.einsum("bqhe,bkhe->bhqk", query_norm, key_norm, precision=lax.Precision.HIGHEST)
        * score_scale
    )
    exponent = jnp.exp(scores)
    attn_weights = exponent / jnp.sum(exponent, -1, keepdims=True)
    return jnp.einsum("bhqk,bkhe->bqhe", attn_weights, value_rows, precision=lax.Precision.HIGHEST)


def cross_rows(left, right):
    return lax.dot_general(
        left, right, (((1,), (1,)), ((), ())), preferred_element_type=jnp.float32
    )


def over_tokens(left, right):
    return lax.dot_general(
        left, right, (((0,), (0,)), ((), ())), preferred_element_type=jnp.float32
    )


def body(tokens, weights, direction, precision):
    model_width = tokens.shape[1]
    local_rows = tokens.shape[0]
    share_rows = weights.shape[0]
    head_cols = weights.shape[2]
    normed = layer_norm(tokens.astype(jnp.float32)).astype(jnp.bfloat16)
    local = jnp.concatenate(
        [weights[:, 0:3], direction[:, 0:3], weights[:, 3:4], direction[:, 3:4]], 1
    ).reshape(share_rows, 8 * head_cols)
    gathered = lax.all_gather(local.T, FSDP, axis=1, tiled=True)
    in_both = gathered[: 6 * head_cols]
    out_both = gathered[6 * head_cols :]
    both_in = cross_rows(normed, in_both).astype(jnp.bfloat16)
    projected = both_in[:, : 3 * head_cols]
    tangent_in = both_in[:, 3 * head_cols :]

    def to_heads(block):
        return block.astype(jnp.float32).reshape(
            local_rows // PATCHES, PATCHES, 3, head_cols // HEAD, HEAD
        )

    primal = to_heads(projected)
    tangent_heads = to_heads(tangent_in)
    primal_args = (primal[:, :, 0], primal[:, :, 1], primal[:, :, 2])
    tangent_args = (tangent_heads[:, :, 0], tangent_heads[:, :, 1], tangent_heads[:, :, 2])
    mixed, mixed_dot = jax.jvp(attend, primal_args, tangent_args)
    mixed_rows = mixed.reshape(local_rows, head_cols).astype(jnp.bfloat16)
    tangent_out = mixed_dot.reshape(local_rows, head_cols).astype(jnp.bfloat16)
    partial_sum = lax.dot_general(
        jnp.concatenate([tangent_out, mixed_rows], 1),
        out_both,
        (((1,), (0,)), ((), ())),
        preferred_element_type=jnp.float32,
    )
    n_tensor = lax.axis_size(TENSOR)
    chunk = model_width // n_tensor
    arrived = lax.all_to_all(
        partial_sum.astype(jnp.bfloat16).reshape(local_rows, n_tensor, chunk), TENSOR, 1, 1
    )
    output_dot = jnp.sum(arrived.astype(jnp.float32), 1)
    own_precision = lax.dynamic_slice_in_dim(precision, lax.axis_index(TENSOR) * chunk, chunk)
    cotangent_part = (own_precision * output_dot).astype(jnp.bfloat16)
    spread = jnp.broadcast_to(cotangent_part[None], (n_tensor, local_rows, chunk))
    cotangent = jnp.moveaxis(lax.all_to_all(spread, TENSOR, 0, 0), 0, 1).reshape(
        local_rows, model_width
    )
    back_rows = cross_rows(cotangent, out_both[:head_cols])
    back_rows = back_rows.reshape(local_rows // PATCHES, PATCHES, head_cols // HEAD, HEAD)
    primal_out, pullback = jax.vjp(attend, *primal_args)
    gradients = pullback(back_rows)
    stacked = jnp.stack(gradients, axis=2).reshape(local_rows, 3 * head_cols).astype(jnp.bfloat16)
    summed = jnp.concatenate(
        [
            over_tokens(normed, stacked).reshape(model_width, 3, head_cols),
            over_tokens(cotangent, mixed_rows)[:, None, :],
        ],
        axis=1,
    ).astype(jnp.bfloat16)
    n_hi = lax.axis_size("z_hi")
    n_x = lax.axis_size("x")
    summed = summed.reshape(n_hi, n_x, share_rows, 4, head_cols).swapaxes(0, 1)
    summed = summed.reshape(model_width, 4, head_cols)
    summed = lax.psum_scatter(summed, "x", scatter_dimension=0, tiled=True)
    return lax.psum_scatter(summed, "z_hi", scatter_dimension=0, tiled=True).astype(jnp.float32)


def solution(mesh):
    n_fsdp, n_tensor = mesh.devices.shape
    n_x = 4 if n_fsdp % 4 == 0 else n_fsdp
    parts = mesh.devices.reshape(n_fsdp // n_x, n_x, 2, n_tensor // 4, 2)
    fine = Mesh(parts, ("z_hi", "x", "z_lo", "y", "core"))
    return jax.shard_map(
        body,
        mesh=fine,
        in_specs=(P(FSDP, None), P(FSDP, None, TENSOR), P(FSDP, None, TENSOR), P()),
        out_specs=P(FSDP, None, TENSOR),
        check_vma=False,
    )
```

```python
import jax
import jax.numpy as jnp
from jax import lax
from jax.sharding import Mesh, PartitionSpec as P

FSDP = ("z_hi", "x")
TENSOR = ("z_lo", "y", "core")

HEAD = 128
PATCHES = 256


def layer_norm(rows):
    mean_row = jnp.mean(rows, -1, keepdims=True)
    centred = rows - mean_row
    spread = jnp.mean(centred * centred, -1, keepdims=True)
    return centred * lax.rsqrt(spread + 1e-06)


def attend(queries, key_rows, value_rows):
    query_norm = layer_norm(queries)
    key_norm = layer_norm(key_rows)
    score_scale = queries.shape[-1] ** (-0.5)
    scores = (
        jnp.einsum("bqhe,bkhe->bhqk", query_norm, key_norm, precision=lax.Precision.HIGHEST)
        * score_scale
    )
    exponent = jnp.exp(scores)
    attn_weights = exponent / jnp.sum(exponent, -1, keepdims=True)
    return jnp.einsum("bhqk,bkhe->bqhe", attn_weights, value_rows, precision=lax.Precision.HIGHEST)


def cross_rows(left, right):
    return lax.dot_general(
        left, right, (((1,), (1,)), ((), ())), preferred_element_type=jnp.float32
    )


def over_tokens(left, right):
    return lax.dot_general(
        left, right, (((0,), (0,)), ((), ())), preferred_element_type=jnp.float32
    )


def body(tokens, weights, direction, precision):
    model_width = tokens.shape[1]
    local_rows = tokens.shape[0]
    share_rows = weights.shape[0]
    head_cols = weights.shape[2]
    normed = layer_norm(tokens.astype(jnp.float32)).astype(jnp.bfloat16)
    local = jnp.concatenate(
        [weights[:, 0:3], direction[:, 0:3], weights[:, 3:4], direction[:, 3:4]], 1
    ).reshape(share_rows, 8 * head_cols)
    gathered = lax.all_gather(local.T, FSDP, axis=1, tiled=True)
    in_both = gathered[: 6 * head_cols]
    out_both = gathered[6 * head_cols :]
    both_in = cross_rows(normed, in_both).astype(jnp.bfloat16)
    projected = both_in[:, : 3 * head_cols]
    tangent_in = both_in[:, 3 * head_cols :]

    def to_heads(block):
        return block.astype(jnp.float32).reshape(
            local_rows // PATCHES, PATCHES, 3, head_cols // HEAD, HEAD
        )

    primal = to_heads(projected)
    tangent_heads = to_heads(tangent_in)
    primal_args = (primal[:, :, 0], primal[:, :, 1], primal[:, :, 2])
    tangent_args = (tangent_heads[:, :, 0], tangent_heads[:, :, 1], tangent_heads[:, :, 2])
    mixed, mixed_dot = jax.jvp(attend, primal_args, tangent_args)
    mixed_rows = mixed.reshape(local_rows, head_cols).astype(jnp.bfloat16)
    tangent_out = mixed_dot.reshape(local_rows, head_cols).astype(jnp.bfloat16)
    partial_sum = lax.dot_general(
        jnp.concatenate([tangent_out, mixed_rows], 1),
        out_both,
        (((1,), (0,)), ((), ())),
        preferred_element_type=jnp.float32,
    )
    n_tensor = lax.axis_size(TENSOR)
    chunk = model_width // n_tensor
    arrived = lax.all_to_all(
        partial_sum.astype(jnp.bfloat16).reshape(local_rows, n_tensor, chunk), TENSOR, 1, 1
    )
    output_dot = jnp.sum(arrived.astype(jnp.float32), 1)
    own_precision = lax.dynamic_slice_in_dim(precision, lax.axis_index(TENSOR) * chunk, chunk)
    cotangent_part = (own_precision * output_dot).astype(jnp.bfloat16)
    spread = jnp.broadcast_to(cotangent_part[None], (n_tensor, local_rows, chunk))
    cotangent = jnp.moveaxis(lax.all_to_all(spread, TENSOR, 0, 0), 0, 1).reshape(
        local_rows, model_width
    )
    back_rows = cross_rows(cotangent, out_both[:head_cols])
    back_rows = back_rows.reshape(local_rows // PATCHES, PATCHES, head_cols // HEAD, HEAD)
    primal_out, pullback = jax.vjp(attend, *primal_args)
    gradients = pullback(back_rows)
    stacked = jnp.stack(gradients, axis=2).reshape(local_rows, 3 * head_cols).astype(jnp.bfloat16)
    summed = jnp.concatenate(
        [
            over_tokens(normed, stacked).reshape(model_width, 3, head_cols),
            over_tokens(cotangent, mixed_rows)[:, None, :],
        ],
        axis=1,
    ).astype(jnp.bfloat16)
    n_hi = lax.axis_size("z_hi")
    n_x = lax.axis_size("x")
    summed = summed.reshape(n_hi, n_x, share_rows, 4, head_cols).swapaxes(0, 1)
    summed = summed.reshape(model_width, 4, head_cols)
    summed = lax.psum_scatter(summed, "x", scatter_dimension=0, tiled=True)
    arrived_rows = lax.all_to_all(
        summed.reshape(n_hi, share_rows, 4, head_cols), "z_hi", 0, 0
    )
    return jnp.sum(arrived_rows.astype(jnp.float32), 0)


def solution(mesh):
    n_fsdp, n_tensor = mesh.devices.shape
    n_x = 4 if n_fsdp % 4 == 0 else n_fsdp
    parts = mesh.devices.reshape(n_fsdp // n_x, n_x, 2, n_tensor // 4, 2)
    fine = Mesh(parts, ("z_hi", "x", "z_lo", "y", "core"))
    return jax.shard_map(
        body,
        mesh=fine,
        in_specs=(P(FSDP, None), P(FSDP, None, TENSOR), P(FSDP, None, TENSOR), P()),
        out_specs=P(FSDP, None, TENSOR),
        check_vma=False,
    )
```

```python
import jax
import jax.numpy as jnp
from jax import lax
from jax.sharding import Mesh, PartitionSpec as P

FSDP = ("z_hi", "x")
TENSOR = ("z_lo", "y", "core")

HEAD = 128
PATCHES = 256


def layer_norm(rows):
    mean_row = jnp.mean(rows, -1, keepdims=True)
    centred = rows - mean_row
    spread = jnp.mean(centred * centred, -1, keepdims=True)
    return centred * lax.rsqrt(spread + 1e-06)


def attend(queries, key_rows, value_rows):
    query_norm = layer_norm(queries)
    key_norm = layer_norm(key_rows)
    score_scale = queries.shape[-1] ** (-0.5)
    scores = (
        jnp.einsum("bqhe,bkhe->bhqk", query_norm, key_norm, precision=lax.Precision.HIGHEST)
        * score_scale
    )
    exponent = jnp.exp(scores)
    attn_weights = exponent / jnp.sum(exponent, -1, keepdims=True)
    return jnp.einsum("bhqk,bkhe->bqhe", attn_weights, value_rows, precision=lax.Precision.HIGHEST)


def cross_rows(left, right):
    return lax.dot_general(
        left, right, (((1,), (1,)), ((), ())), preferred_element_type=jnp.float32
    )


def over_tokens(left, right):
    return lax.dot_general(
        left, right, (((0,), (0,)), ((), ())), preferred_element_type=jnp.float32
    )


def body(tokens, weights, direction, precision):
    model_width = tokens.shape[1]
    local_rows = tokens.shape[0]
    share_rows = weights.shape[0]
    head_cols = weights.shape[2]
    normed = layer_norm(tokens.astype(jnp.float32)).astype(jnp.bfloat16)
    local = jnp.concatenate(
        [weights[:, 0:3], direction[:, 0:3], weights[:, 3:4], direction[:, 3:4]], 1
    ).reshape(share_rows, 8 * head_cols)
    gathered = lax.all_gather(local.T, FSDP, axis=1, tiled=True)
    in_both = gathered[: 6 * head_cols]
    out_both = gathered[6 * head_cols :]
    both_in = cross_rows(normed, in_both).astype(jnp.bfloat16)
    projected = both_in[:, : 3 * head_cols]
    tangent_in = both_in[:, 3 * head_cols :]

    def to_heads(block):
        return block.astype(jnp.float32).reshape(
            local_rows // PATCHES, PATCHES, 3, head_cols // HEAD, HEAD
        )

    primal = to_heads(projected)
    tangent_heads = to_heads(tangent_in)
    primal_args = (primal[:, :, 0], primal[:, :, 1], primal[:, :, 2])
    tangent_args = (tangent_heads[:, :, 0], tangent_heads[:, :, 1], tangent_heads[:, :, 2])
    mixed, mixed_dot = jax.jvp(attend, primal_args, tangent_args)
    mixed_rows = mixed.reshape(local_rows, head_cols).astype(jnp.bfloat16)
    tangent_out = mixed_dot.reshape(local_rows, head_cols).astype(jnp.bfloat16)
    partial_cols = lax.dot_general(
        out_both,
        jnp.concatenate([tangent_out, mixed_rows], 1),
        (((0,), (1,)), ((), ())),
        preferred_element_type=jnp.float32,
    )
    n_tensor = lax.axis_size(TENSOR)
    chunk = model_width // n_tensor
    arrived = lax.all_to_all(
        partial_cols.astype(jnp.bfloat16).reshape(n_tensor, chunk, local_rows), TENSOR, 0, 0
    )
    output_dot = jnp.sum(arrived.astype(jnp.float32), 0)
    own_precision = lax.dynamic_slice_in_dim(precision, lax.axis_index(TENSOR) * chunk, chunk)
    cotangent_part = (own_precision[:, None] * output_dot).astype(jnp.bfloat16)
    spread = jnp.broadcast_to(cotangent_part[None], (n_tensor, chunk, local_rows))
    cotangent_cols = lax.all_to_all(spread, TENSOR, 0, 0).reshape(model_width, local_rows)
    back_rows = lax.dot_general(
        cotangent_cols, out_both[:head_cols], (((0,), (1,)), ((), ())),
        preferred_element_type=jnp.float32,
    )
    back_rows = back_rows.reshape(local_rows // PATCHES, PATCHES, head_cols // HEAD, HEAD)
    primal_out, pullback = jax.vjp(attend, *primal_args)
    gradients = pullback(back_rows)
    stacked = jnp.stack(gradients, axis=2).reshape(local_rows, 3 * head_cols).astype(jnp.bfloat16)
    summed = jnp.concatenate(
        [
            over_tokens(normed, stacked).reshape(model_width, 3, head_cols),
            jnp.dot(cotangent_cols, mixed_rows, preferred_element_type=jnp.float32)[:, None, :],
        ],
        axis=1,
    ).astype(jnp.bfloat16)
    n_hi = lax.axis_size("z_hi")
    n_x = lax.axis_size("x")
    summed = summed.reshape(n_hi, n_x, share_rows, 4, head_cols).swapaxes(0, 1)
    summed = summed.reshape(model_width, 4, head_cols)
    summed = lax.psum_scatter(summed, "x", scatter_dimension=0, tiled=True)
    return lax.psum_scatter(summed, "z_hi", scatter_dimension=0, tiled=True).astype(jnp.float32)


def solution(mesh):
    n_fsdp, n_tensor = mesh.devices.shape
    n_x = 4 if n_fsdp % 4 == 0 else n_fsdp
    parts = mesh.devices.reshape(n_fsdp // n_x, n_x, 2, n_tensor // 4, 2)
    fine = Mesh(parts, ("z_hi", "x", "z_lo", "y", "core"))
    return jax.shard_map(
        body,
        mesh=fine,
        in_specs=(P(FSDP, None), P(FSDP, None, TENSOR), P(FSDP, None, TENSOR), P()),
        out_specs=P(FSDP, None, TENSOR),
        check_vma=False,
    )
```

```python
import jax
import jax.numpy as jnp
from jax import lax
from jax.sharding import Mesh, PartitionSpec as P

FSDP = ("z_hi", "x")
TENSOR = ("z_lo", "y", "core")

HEAD = 128
PATCHES = 256


def layer_norm(rows):
    mean_row = jnp.mean(rows, -1, keepdims=True)
    centred = rows - mean_row
    spread = jnp.mean(centred * centred, -1, keepdims=True)
    return centred * lax.rsqrt(spread + 1e-06)


def attend(queries, key_rows, value_rows):
    query_norm = layer_norm(queries)
    key_norm = layer_norm(key_rows)
    score_scale = queries.shape[-1] ** (-0.5)
    scores = (
        jnp.einsum("bqhe,bkhe->bhqk", query_norm, key_norm, precision=lax.Precision.HIGHEST)
        * score_scale
    )
    exponent = jnp.exp(scores)
    attn_weights = exponent / jnp.sum(exponent, -1, keepdims=True)
    return jnp.einsum("bhqk,bkhe->bqhe", attn_weights, value_rows, precision=lax.Precision.HIGHEST)


def cross_rows(left, right):
    return lax.dot_general(
        left, right, (((1,), (1,)), ((), ())), preferred_element_type=jnp.float32
    )


def over_tokens(left, right):
    return lax.dot_general(
        left, right, (((0,), (0,)), ((), ())), preferred_element_type=jnp.float32
    )


def body(tokens, weights, direction, precision):
    model_width = tokens.shape[1]
    local_rows = tokens.shape[0]
    share_rows = weights.shape[0]
    head_cols = weights.shape[2]
    normed = layer_norm(tokens.astype(jnp.float32)).astype(jnp.bfloat16)
    local = jnp.concatenate(
        [weights[:, 0:3], direction[:, 0:3], weights[:, 3:4], direction[:, 3:4]], 1
    ).reshape(share_rows, 8 * head_cols)
    gathered = lax.all_gather(local.T, FSDP, axis=1, tiled=True)
    in_both = gathered[: 6 * head_cols]
    out_both = gathered[6 * head_cols :]
    both_in = cross_rows(normed, in_both).astype(jnp.bfloat16)
    projected = both_in[:, : 3 * head_cols]
    tangent_in = both_in[:, 3 * head_cols :]

    def to_heads(block):
        return block.astype(jnp.float32).reshape(
            local_rows // PATCHES, PATCHES, 3, head_cols // HEAD, HEAD
        )

    primal = to_heads(projected)
    tangent_heads = to_heads(tangent_in)
    primal_args = (primal[:, :, 0], primal[:, :, 1], primal[:, :, 2])
    tangent_args = (tangent_heads[:, :, 0], tangent_heads[:, :, 1], tangent_heads[:, :, 2])
    mixed, mixed_dot = jax.jvp(attend, primal_args, tangent_args)
    mixed_rows = mixed.reshape(local_rows, head_cols).astype(jnp.bfloat16)
    tangent_out = mixed_dot.reshape(local_rows, head_cols).astype(jnp.bfloat16)
    partial_cols = lax.dot_general(
        out_both,
        jnp.concatenate([tangent_out, mixed_rows], 1),
        (((0,), (1,)), ((), ())),
        preferred_element_type=jnp.float32,
    )
    n_tensor = lax.axis_size(TENSOR)
    chunk = model_width // n_tensor
    n_core = lax.axis_size("core")
    n_chip = n_tensor // n_core
    by_core = (
        partial_cols.astype(jnp.bfloat16)
        .reshape(n_chip, n_core, chunk, local_rows)
        .swapaxes(0, 1)
    )
    pair_sum = jnp.sum(lax.all_to_all(by_core, "core", 0, 0).astype(jnp.float32), 0)
    arrived = lax.all_to_all(pair_sum.astype(jnp.bfloat16), ("z_lo", "y"), 0, 0)
    output_dot = jnp.sum(arrived.astype(jnp.float32), 0)
    own_precision = lax.dynamic_slice_in_dim(precision, lax.axis_index(TENSOR) * chunk, chunk)
    cotangent_part = (own_precision[:, None] * output_dot).astype(jnp.bfloat16)
    spread = jnp.broadcast_to(cotangent_part[None], (n_chip, chunk, local_rows))
    on_chip = lax.all_to_all(spread, ("z_lo", "y"), 0, 0)
    spread = jnp.broadcast_to(on_chip[None], (n_core, n_chip, chunk, local_rows))
    cotangent_cols = (
        lax.all_to_all(spread, "core", 0, 0).swapaxes(0, 1).reshape(model_width, local_rows)
    )
    back_rows = lax.dot_general(
        cotangent_cols, out_both[:head_cols], (((0,), (1,)), ((), ())),
        preferred_element_type=jnp.float32,
    )
    back_rows = back_rows.reshape(local_rows // PATCHES, PATCHES, head_cols // HEAD, HEAD)
    primal_out, pullback = jax.vjp(attend, *primal_args)
    gradients = pullback(back_rows)
    stacked = jnp.stack(gradients, axis=2).reshape(local_rows, 3 * head_cols).astype(jnp.bfloat16)
    summed = jnp.concatenate(
        [
            over_tokens(normed, stacked).reshape(model_width, 3, head_cols),
            jnp.dot(cotangent_cols, mixed_rows, preferred_element_type=jnp.float32)[:, None, :],
        ],
        axis=1,
    ).astype(jnp.bfloat16)
    n_hi = lax.axis_size("z_hi")
    n_x = lax.axis_size("x")
    summed = summed.reshape(n_hi, n_x, share_rows, 4, head_cols).swapaxes(0, 1)
    summed = summed.reshape(model_width, 4, head_cols)
    summed = lax.psum_scatter(summed, "x", scatter_dimension=0, tiled=True)
    return lax.psum_scatter(summed, "z_hi", scatter_dimension=0, tiled=True).astype(jnp.float32)


def solution(mesh):
    n_fsdp, n_tensor = mesh.devices.shape
    n_x = 4 if n_fsdp % 4 == 0 else n_fsdp
    parts = mesh.devices.reshape(n_fsdp // n_x, n_x, 2, n_tensor // 4, 2)
    fine = Mesh(parts, ("z_hi", "x", "z_lo", "y", "core"))
    return jax.shard_map(
        body,
        mesh=fine,
        in_specs=(P(FSDP, None), P(FSDP, None, TENSOR), P(FSDP, None, TENSOR), P()),
        out_specs=P(FSDP, None, TENSOR),
        check_vma=False,
    )
```

```python
import jax
import jax.numpy as jnp
from jax import lax
from jax.sharding import Mesh, PartitionSpec as P

FSDP = ("z_hi", "x")
TENSOR = ("z_lo", "y", "core")

HEAD = 128
PATCHES = 256


def layer_norm(rows):
    mean_row = jnp.mean(rows, -1, keepdims=True)
    centred = rows - mean_row
    spread = jnp.mean(centred * centred, -1, keepdims=True)
    return centred * lax.rsqrt(spread + 1e-06)


def attend(queries, key_rows, value_rows):
    query_norm = layer_norm(queries)
    key_norm = layer_norm(key_rows)
    score_scale = queries.shape[-1] ** (-0.5)
    scores = (
        jnp.einsum("bqhe,bkhe->bhqk", query_norm, key_norm, precision=lax.Precision.HIGHEST)
        * score_scale
    )
    exponent = jnp.exp(scores)
    attn_weights = exponent / jnp.sum(exponent, -1, keepdims=True)
    return jnp.einsum("bhqk,bkhe->bqhe", attn_weights, value_rows, precision=lax.Precision.HIGHEST)


def cross_rows(left, right):
    return lax.dot_general(
        left, right, (((1,), (1,)), ((), ())), preferred_element_type=jnp.float32
    )


def over_tokens(left, right):
    return lax.dot_general(
        left, right, (((0,), (0,)), ((), ())), preferred_element_type=jnp.float32
    )


def body(tokens, weights, direction, precision):
    model_width = tokens.shape[1]
    local_rows = tokens.shape[0]
    share_rows = weights.shape[0]
    head_cols = weights.shape[2]
    normed = layer_norm(tokens.astype(jnp.float32)).astype(jnp.bfloat16)
    local = jnp.concatenate(
        [weights[:, 0:3], direction[:, 0:3], weights[:, 3:4], direction[:, 3:4]], 1
    ).reshape(share_rows, 8 * head_cols)
    gathered = lax.all_gather(local.T, FSDP, axis=1, tiled=True)
    in_both = gathered[: 6 * head_cols]
    out_both = gathered[6 * head_cols :]
    both_in = cross_rows(normed, in_both).astype(jnp.bfloat16)
    projected = both_in[:, : 3 * head_cols]
    tangent_in = both_in[:, 3 * head_cols :]

    def to_heads(block):
        return block.astype(jnp.float32).reshape(
            local_rows // PATCHES, PATCHES, 3, head_cols // HEAD, HEAD
        )

    primal = to_heads(projected)
    tangent_heads = to_heads(tangent_in)
    primal_args = (primal[:, :, 0], primal[:, :, 1], primal[:, :, 2])
    tangent_args = (tangent_heads[:, :, 0], tangent_heads[:, :, 1], tangent_heads[:, :, 2])
    mixed, mixed_dot = jax.jvp(attend, primal_args, tangent_args)
    mixed_rows = mixed.reshape(local_rows, head_cols).astype(jnp.bfloat16)
    tangent_out = mixed_dot.reshape(local_rows, head_cols).astype(jnp.bfloat16)
    partial_cols = lax.dot_general(
        out_both,
        jnp.concatenate([tangent_out, mixed_rows], 1),
        (((0,), (1,)), ((), ())),
        preferred_element_type=jnp.float32,
    )
    n_tensor = lax.axis_size(TENSOR)
    chunk = model_width // n_tensor
    n_core = lax.axis_size("core")
    n_chip = n_tensor // n_core
    by_core = (
        partial_cols.astype(jnp.bfloat16)
        .reshape(n_chip, n_core, chunk, local_rows)
        .swapaxes(0, 1)
    )
    pair_sum = jnp.sum(lax.all_to_all(by_core, "core", 0, 0).astype(jnp.float32), 0)
    arrived = lax.all_to_all(pair_sum.astype(jnp.bfloat16), ("z_lo", "y"), 0, 0)
    output_dot = jnp.sum(arrived.astype(jnp.float32), 0)
    own_precision = lax.dynamic_slice_in_dim(precision, lax.axis_index(TENSOR) * chunk, chunk)
    cotangent_part = (own_precision[:, None] * output_dot).astype(jnp.bfloat16)
    spread = jnp.broadcast_to(cotangent_part[None], (n_chip, chunk, local_rows))
    on_chip = lax.all_to_all(spread, ("z_lo", "y"), 0, 0)
    spread = jnp.broadcast_to(on_chip[None], (n_core, n_chip, chunk, local_rows))
    cotangent_cols = (
        lax.all_to_all(spread, "core", 0, 0).swapaxes(0, 1).reshape(model_width, local_rows)
    )
    back_rows = lax.dot_general(
        cotangent_cols, out_both[:head_cols], (((0,), (1,)), ((), ())),
        preferred_element_type=jnp.float32,
    )
    back_rows = back_rows.reshape(local_rows // PATCHES, PATCHES, head_cols // HEAD, HEAD)
    primal_out, pullback = jax.vjp(attend, *primal_args)
    gradients = pullback(back_rows)
    stacked = jnp.stack(gradients, axis=2).reshape(local_rows, 3 * head_cols).astype(jnp.bfloat16)
    summed = jnp.concatenate(
        [
            over_tokens(normed, stacked).reshape(model_width, 3, head_cols),
            jnp.dot(cotangent_cols, mixed_rows, preferred_element_type=jnp.float32)[:, None, :],
        ],
        axis=1,
    ).astype(jnp.bfloat16)
    n_hi = lax.axis_size("z_hi")
    n_x = lax.axis_size("x")
    summed = summed.reshape(n_hi, n_x, share_rows, 4, head_cols).swapaxes(0, 1)
    summed = summed.reshape(model_width, 4, head_cols)
    arrived_x = lax.all_to_all(summed.reshape(n_x, n_hi * share_rows, 4, head_cols), "x", 0, 0)
    summed = jnp.sum(arrived_x.astype(jnp.float32), 0).astype(jnp.bfloat16)
    arrived_rows = lax.all_to_all(summed.reshape(n_hi, share_rows, 4, head_cols), "z_hi", 0, 0)
    return jnp.sum(arrived_rows.astype(jnp.float32), 0)


def solution(mesh):
    n_fsdp, n_tensor = mesh.devices.shape
    n_x = 4 if n_fsdp % 4 == 0 else n_fsdp
    parts = mesh.devices.reshape(n_fsdp // n_x, n_x, 2, n_tensor // 4, 2)
    fine = Mesh(parts, ("z_hi", "x", "z_lo", "y", "core"))
    return jax.shard_map(
        body,
        mesh=fine,
        in_specs=(P(FSDP, None), P(FSDP, None, TENSOR), P(FSDP, None, TENSOR), P()),
        out_specs=P(FSDP, None, TENSOR),
        check_vma=False,
    )
```

```python
import jax
import jax.numpy as jnp
from jax import lax
from jax.sharding import Mesh, PartitionSpec as P

FSDP = ("z_hi", "x")
TENSOR = ("z_lo", "y", "core")

HEAD = 128
PATCHES = 256


def layer_norm(rows):
    mean_row = jnp.mean(rows, -1, keepdims=True)
    centred = rows - mean_row
    spread = jnp.mean(centred * centred, -1, keepdims=True)
    return centred * lax.rsqrt(spread + 1e-06)


def attend(queries, key_rows, value_rows):
    query_norm = layer_norm(queries)
    key_norm = layer_norm(key_rows)
    score_scale = queries.shape[-1] ** (-0.5)
    scores = (
        jnp.einsum("bqhe,bkhe->bhqk", query_norm, key_norm, precision=lax.Precision.HIGHEST)
        * score_scale
    )
    exponent = jnp.exp(scores)
    attn_weights = exponent / jnp.sum(exponent, -1, keepdims=True)
    return jnp.einsum("bhqk,bkhe->bqhe", attn_weights, value_rows, precision=lax.Precision.HIGHEST)


def cross_rows(left, right):
    return lax.dot_general(
        left, right, (((1,), (1,)), ((), ())), preferred_element_type=jnp.float32
    )


def over_tokens(left, right):
    return lax.dot_general(
        left, right, (((0,), (0,)), ((), ())), preferred_element_type=jnp.float32
    )


def body(tokens, weights, direction, precision):
    model_width = tokens.shape[1]
    local_rows = tokens.shape[0]
    share_rows = weights.shape[0]
    head_cols = weights.shape[2]
    normed = layer_norm(tokens.astype(jnp.float32)).astype(jnp.bfloat16)
    local = jnp.concatenate(
        [weights[:, 0:3], direction[:, 0:3], weights[:, 3:4], direction[:, 3:4]], 1
    ).reshape(share_rows, 8 * head_cols)
    gathered = lax.all_gather(local.T, FSDP, axis=1, tiled=True)
    in_both = gathered[: 6 * head_cols]
    out_both = gathered[6 * head_cols :]
    both_in = cross_rows(normed, in_both).astype(jnp.bfloat16)
    projected = both_in[:, : 3 * head_cols]
    tangent_in = both_in[:, 3 * head_cols :]

    def to_heads(block):
        return block.astype(jnp.float32).reshape(
            local_rows // PATCHES, PATCHES, 3, head_cols // HEAD, HEAD
        )

    primal = to_heads(projected)
    tangent_heads = to_heads(tangent_in)
    primal_args = (primal[:, :, 0], primal[:, :, 1], primal[:, :, 2])
    tangent_args = (tangent_heads[:, :, 0], tangent_heads[:, :, 1], tangent_heads[:, :, 2])
    mixed, mixed_dot = jax.jvp(attend, primal_args, tangent_args)
    mixed_rows = mixed.reshape(local_rows, head_cols).astype(jnp.bfloat16)
    tangent_out = mixed_dot.reshape(local_rows, head_cols).astype(jnp.bfloat16)
    partial_cols = lax.dot_general(
        out_both,
        jnp.concatenate([tangent_out, mixed_rows], 1),
        (((0,), (1,)), ((), ())),
        preferred_element_type=jnp.float32,
    )
    n_tensor = lax.axis_size(TENSOR)
    chunk = model_width // n_tensor
    n_core = lax.axis_size("core")
    n_chip = n_tensor // n_core
    swap = [(0, 1), (1, 0)]
    core_index = lax.axis_index("core")
    by_core = partial_cols.astype(jnp.bfloat16).reshape(n_chip, n_core, chunk, local_rows)
    kept = lax.dynamic_index_in_dim(by_core, core_index, 1, keepdims=False)
    given = lax.dynamic_index_in_dim(by_core, 1 - core_index, 1, keepdims=False)
    received = lax.ppermute(given, "core", swap)
    pair_sum = kept.astype(jnp.float32) + received.astype(jnp.float32)
    arrived = lax.all_to_all(pair_sum.astype(jnp.bfloat16), ("z_lo", "y"), 0, 0)
    output_dot = jnp.sum(arrived.astype(jnp.float32), 0)
    own_precision = lax.dynamic_slice_in_dim(precision, lax.axis_index(TENSOR) * chunk, chunk)
    cotangent_part = (own_precision[:, None] * output_dot).astype(jnp.bfloat16)
    spread = jnp.broadcast_to(cotangent_part[None], (n_chip, chunk, local_rows))
    on_chip = lax.all_to_all(spread, ("z_lo", "y"), 0, 0)
    partner = lax.ppermute(on_chip, "core", swap)
    first = core_index == 0
    cotangent_cols = jnp.stack(
        [jnp.where(first, on_chip, partner), jnp.where(first, partner, on_chip)], 1
    ).reshape(model_width, local_rows)
    back_rows = lax.dot_general(
        cotangent_cols, out_both[:head_cols], (((0,), (1,)), ((), ())),
        preferred_element_type=jnp.float32,
    )
    back_rows = back_rows.reshape(local_rows // PATCHES, PATCHES, head_cols // HEAD, HEAD)
    primal_out, pullback = jax.vjp(attend, *primal_args)
    gradients = pullback(back_rows)
    stacked = jnp.stack(gradients, axis=2).reshape(local_rows, 3 * head_cols).astype(jnp.bfloat16)
    summed = jnp.concatenate(
        [
            over_tokens(normed, stacked).reshape(model_width, 3, head_cols),
            jnp.dot(cotangent_cols, mixed_rows, preferred_element_type=jnp.float32)[:, None, :],
        ],
        axis=1,
    ).astype(jnp.bfloat16)
    n_hi = lax.axis_size("z_hi")
    n_x = lax.axis_size("x")
    summed = summed.reshape(n_hi, n_x, share_rows, 4, head_cols).swapaxes(0, 1)
    summed = summed.reshape(model_width, 4, head_cols)
    summed = lax.psum_scatter(summed, "x", scatter_dimension=0, tiled=True)
    return lax.psum_scatter(summed, "z_hi", scatter_dimension=0, tiled=True).astype(jnp.float32)


def solution(mesh):
    n_fsdp, n_tensor = mesh.devices.shape
    n_x = 4 if n_fsdp % 4 == 0 else n_fsdp
    parts = mesh.devices.reshape(n_fsdp // n_x, n_x, 2, n_tensor // 4, 2)
    fine = Mesh(parts, ("z_hi", "x", "z_lo", "y", "core"))
    return jax.shard_map(
        body,
        mesh=fine,
        in_specs=(P(FSDP, None), P(FSDP, None, TENSOR), P(FSDP, None, TENSOR), P()),
        out_specs=P(FSDP, None, TENSOR),
        check_vma=False,
    )
```

```python
import jax
import jax.numpy as jnp
from jax import lax
from jax.sharding import Mesh, PartitionSpec as P

FSDP = ("z_hi", "x")
TENSOR = ("z_lo", "y", "core")

HEAD = 128
PATCHES = 256


def layer_norm(rows):
    mean_row = jnp.mean(rows, -1, keepdims=True)
    centred = rows - mean_row
    spread = jnp.mean(centred * centred, -1, keepdims=True)
    return centred * lax.rsqrt(spread + 1e-06)


def attend(queries, key_rows, value_rows):
    query_norm = layer_norm(queries)
    key_norm = layer_norm(key_rows)
    score_scale = queries.shape[-1] ** (-0.5)
    scores = (
        jnp.einsum("bqhe,bkhe->bhqk", query_norm, key_norm, precision=lax.Precision.HIGHEST)
        * score_scale
    )
    exponent = jnp.exp(scores)
    attn_weights = exponent / jnp.sum(exponent, -1, keepdims=True)
    return jnp.einsum("bhqk,bkhe->bqhe", attn_weights, value_rows, precision=lax.Precision.HIGHEST)


def cross_rows(left, right):
    return lax.dot_general(
        left, right, (((1,), (1,)), ((), ())), preferred_element_type=jnp.float32
    )


def over_tokens(left, right):
    return lax.dot_general(
        left, right, (((0,), (0,)), ((), ())), preferred_element_type=jnp.float32
    )


def body(tokens, weights, direction, precision):
    model_width = tokens.shape[1]
    local_rows = tokens.shape[0]
    share_rows = weights.shape[0]
    head_cols = weights.shape[2]
    normed = layer_norm(tokens.astype(jnp.float32)).astype(jnp.bfloat16)
    local = jnp.concatenate(
        [weights[:, 0:3], direction[:, 0:3], weights[:, 3:4], direction[:, 3:4]], 1
    ).reshape(share_rows, 8 * head_cols)
    gathered = lax.all_gather(local.T, FSDP, axis=1, tiled=True)
    in_both = gathered[: 6 * head_cols]
    out_both = gathered[6 * head_cols :]
    both_in = cross_rows(normed, in_both).astype(jnp.bfloat16)
    projected = both_in[:, : 3 * head_cols]
    tangent_in = both_in[:, 3 * head_cols :]

    def to_heads(block):
        return block.astype(jnp.float32).reshape(
            local_rows // PATCHES, PATCHES, 3, head_cols // HEAD, HEAD
        )

    primal = to_heads(projected)
    tangent_heads = to_heads(tangent_in)
    primal_args = (primal[:, :, 0], primal[:, :, 1], primal[:, :, 2])
    tangent_args = (tangent_heads[:, :, 0], tangent_heads[:, :, 1], tangent_heads[:, :, 2])
    mixed, mixed_dot = jax.jvp(attend, primal_args, tangent_args)
    mixed_rows = mixed.reshape(local_rows, head_cols).astype(jnp.bfloat16)
    tangent_out = mixed_dot.reshape(local_rows, head_cols).astype(jnp.bfloat16)
    partial_cols = lax.dot_general(
        out_both,
        jnp.concatenate([tangent_out, mixed_rows], 1),
        (((0,), (1,)), ((), ())),
        preferred_element_type=jnp.float32,
    )
    n_tensor = lax.axis_size(TENSOR)
    chunk = model_width // n_tensor
    n_core = lax.axis_size("core")
    n_chip = n_tensor // n_core
    swap = [(0, 1), (1, 0)]
    core_index = lax.axis_index("core")
    by_core = partial_cols.astype(jnp.bfloat16).reshape(n_chip, n_core, chunk, local_rows)
    kept = lax.dynamic_index_in_dim(by_core, core_index, 1, keepdims=False)
    given = lax.dynamic_index_in_dim(by_core, 1 - core_index, 1, keepdims=False)
    received = lax.ppermute(given, "core", swap)
    pair_sum = kept.astype(jnp.float32) + received.astype(jnp.float32)
    arrived = lax.all_to_all(pair_sum.astype(jnp.bfloat16), ("z_lo", "y"), 0, 0)
    output_dot = jnp.sum(arrived.astype(jnp.float32), 0)
    own_precision = lax.dynamic_slice_in_dim(precision, lax.axis_index(TENSOR) * chunk, chunk)
    cotangent_part = (own_precision[:, None] * output_dot).astype(jnp.bfloat16)
    spread = jnp.broadcast_to(cotangent_part[None], (n_chip, chunk, local_rows))
    on_chip = lax.all_to_all(spread, ("z_lo", "y"), 0, 0)
    partner = lax.ppermute(on_chip, "core", swap)
    first = core_index == 0
    cotangent_cols = jnp.stack(
        [jnp.where(first, on_chip, partner), jnp.where(first, partner, on_chip)], 1
    ).reshape(model_width, local_rows)
    back_rows = lax.dot_general(
        cotangent_cols, out_both[:head_cols], (((0,), (1,)), ((), ())),
        preferred_element_type=jnp.float32,
    )
    back_rows = back_rows.reshape(local_rows // PATCHES, PATCHES, head_cols // HEAD, HEAD)
    primal_out, pullback = jax.vjp(attend, *primal_args)
    gradients = pullback(back_rows)
    stacked = jnp.stack(gradients, axis=2).reshape(local_rows, 3 * head_cols).astype(jnp.bfloat16)
    summed = jnp.concatenate(
        [
            over_tokens(normed, stacked).reshape(model_width, 3, head_cols),
            jnp.dot(cotangent_cols, mixed_rows, preferred_element_type=jnp.float32)[:, None, :],
        ],
        axis=1,
    ).astype(jnp.bfloat16)
    n_hi = lax.axis_size("z_hi")
    n_x = lax.axis_size("x")
    summed = summed.reshape(n_hi, n_x, share_rows, 4, head_cols).swapaxes(0, 1)
    summed = summed.reshape(model_width, 4, head_cols)
    summed = lax.psum_scatter(summed, "x", scatter_dimension=0, tiled=True)
    blocks = summed.reshape(n_hi, share_rows, 4, head_cols)
    hi_index = lax.axis_index("z_hi")
    total = lax.dynamic_index_in_dim(blocks, hi_index, 0, keepdims=False).astype(jnp.float32)
    for shift in range(1, n_hi):
        outgoing = lax.dynamic_index_in_dim(blocks, (hi_index + shift) % n_hi, 0, keepdims=False)
        pairs = [(i, (i + shift) % n_hi) for i in range(n_hi)]
        total = total + lax.ppermute(outgoing, "z_hi", pairs).astype(jnp.float32)
    return total


def solution(mesh):
    n_fsdp, n_tensor = mesh.devices.shape
    n_x = 4 if n_fsdp % 4 == 0 else n_fsdp
    parts = mesh.devices.reshape(n_fsdp // n_x, n_x, 2, n_tensor // 4, 2)
    fine = Mesh(parts, ("z_hi", "x", "z_lo", "y", "core"))
    return jax.shard_map(
        body,
        mesh=fine,
        in_specs=(P(FSDP, None), P(FSDP, None, TENSOR), P(FSDP, None, TENSOR), P()),
        out_specs=P(FSDP, None, TENSOR),
        check_vma=False,
    )
```

```python
import jax
import jax.numpy as jnp
from jax import lax
from jax.sharding import Mesh, PartitionSpec as P

FSDP = ("z_hi", "x")
TENSOR = ("z_lo", "y", "core")

HEAD = 128
PATCHES = 256


def layer_norm(rows):
    mean_row = jnp.mean(rows, -1, keepdims=True)
    centred = rows - mean_row
    spread = jnp.mean(centred * centred, -1, keepdims=True)
    return centred * lax.rsqrt(spread + 1e-06)


def attend(queries, key_rows, value_rows):
    query_norm = layer_norm(queries)
    key_norm = layer_norm(key_rows)
    score_scale = queries.shape[-1] ** (-0.5)
    scores = (
        jnp.einsum("bqhe,bkhe->bhqk", query_norm, key_norm, precision=lax.Precision.HIGHEST)
        * score_scale
    )
    exponent = jnp.exp(scores)
    attn_weights = exponent / jnp.sum(exponent, -1, keepdims=True)
    return jnp.einsum("bhqk,bkhe->bqhe", attn_weights, value_rows, precision=lax.Precision.HIGHEST)


def cross_rows(left, right):
    return lax.dot_general(
        left, right, (((1,), (1,)), ((), ())), preferred_element_type=jnp.float32
    )


def over_tokens(left, right):
    return lax.dot_general(
        left, right, (((0,), (0,)), ((), ())), preferred_element_type=jnp.float32
    )


def body(tokens, weights, direction, precision):
    model_width = tokens.shape[1]
    local_rows = tokens.shape[0]
    share_rows = weights.shape[0]
    head_cols = weights.shape[2]
    normed = layer_norm(tokens.astype(jnp.float32)).astype(jnp.bfloat16)
    local = jnp.concatenate(
        [weights[:, 0:3], direction[:, 0:3], weights[:, 3:4], direction[:, 3:4]], 1
    ).reshape(share_rows, 8 * head_cols)
    gathered = lax.all_gather(local.T, FSDP, axis=1, tiled=True)
    in_both = gathered[: 6 * head_cols]
    out_both = gathered[6 * head_cols :]
    both_in = cross_rows(normed, in_both).astype(jnp.bfloat16)
    projected = both_in[:, : 3 * head_cols]
    tangent_in = both_in[:, 3 * head_cols :]

    def to_heads(block):
        return block.astype(jnp.float32).reshape(
            local_rows // PATCHES, PATCHES, 3, head_cols // HEAD, HEAD
        )

    primal = to_heads(projected)
    tangent_heads = to_heads(tangent_in)
    primal_args = (primal[:, :, 0], primal[:, :, 1], primal[:, :, 2])
    tangent_args = (tangent_heads[:, :, 0], tangent_heads[:, :, 1], tangent_heads[:, :, 2])
    mixed, mixed_dot = jax.jvp(attend, primal_args, tangent_args)
    mixed_rows = mixed.reshape(local_rows, head_cols).astype(jnp.bfloat16)
    tangent_out = mixed_dot.reshape(local_rows, head_cols).astype(jnp.bfloat16)
    partial_cols = lax.dot_general(
        out_both,
        jnp.concatenate([tangent_out, mixed_rows], 1),
        (((0,), (1,)), ((), ())),
        preferred_element_type=jnp.float32,
    )
    n_tensor = lax.axis_size(TENSOR)
    chunk = model_width // n_tensor
    n_core = lax.axis_size("core")
    n_chip = n_tensor // n_core
    swap = [(0, 1), (1, 0)]
    core_index = lax.axis_index("core")
    by_core = partial_cols.astype(jnp.bfloat16).reshape(n_chip, n_core, chunk, local_rows)
    kept = lax.dynamic_index_in_dim(by_core, core_index, 1, keepdims=False)
    given = lax.dynamic_index_in_dim(by_core, 1 - core_index, 1, keepdims=False)
    received = lax.ppermute(given, "core", swap)
    pair_sum = kept.astype(jnp.float32) + received.astype(jnp.float32)
    arrived = lax.all_to_all(pair_sum.astype(jnp.bfloat16), ("z_lo", "y"), 0, 0)
    output_dot = jnp.sum(arrived.astype(jnp.float32), 0)
    own_precision = lax.dynamic_slice_in_dim(precision, lax.axis_index(TENSOR) * chunk, chunk)
    cotangent_part = (own_precision[:, None] * output_dot).astype(jnp.bfloat16)
    spread = jnp.broadcast_to(cotangent_part[None], (n_chip, chunk, local_rows))
    on_chip = lax.all_to_all(spread, ("z_lo", "y"), 0, 0)
    partner = lax.ppermute(on_chip, "core", swap)
    first = core_index == 0
    cotangent_cols = jnp.stack(
        [jnp.where(first, on_chip, partner), jnp.where(first, partner, on_chip)], 1
    ).reshape(model_width, local_rows)
    back_rows = lax.dot_general(
        cotangent_cols, out_both[:head_cols], (((0,), (1,)), ((), ())),
        preferred_element_type=jnp.float32,
    )
    back_rows = back_rows.reshape(local_rows // PATCHES, PATCHES, head_cols // HEAD, HEAD)
    primal_out, pullback = jax.vjp(attend, *primal_args)
    gradients = pullback(back_rows)
    stacked = jnp.stack(gradients, axis=2).reshape(local_rows, 3 * head_cols).astype(jnp.bfloat16)
    summed = jnp.concatenate(
        [
            over_tokens(normed, stacked).reshape(model_width, 3, head_cols),
            jnp.dot(cotangent_cols, mixed_rows, preferred_element_type=jnp.float32)[:, None, :],
        ],
        axis=1,
    ).astype(jnp.bfloat16)
    n_hi = lax.axis_size("z_hi")
    n_x = lax.axis_size("x")
    summed = summed.reshape(n_hi, n_x, share_rows, 4, head_cols).swapaxes(0, 1)
    summed = summed.reshape(model_width, 4, head_cols)
    summed = lax.psum_scatter(summed, "x", scatter_dimension=0, tiled=True)
    blocks = summed.reshape(n_hi, share_rows, 4, head_cols)
    hi_index = lax.axis_index("z_hi")
    total = lax.dynamic_index_in_dim(blocks, hi_index, 0, keepdims=False).astype(jnp.float32)
    for shift in sorted(range(1, n_hi), key=lambda k: -min(k, n_hi - k)):
        outgoing = lax.dynamic_index_in_dim(blocks, (hi_index + shift) % n_hi, 0, keepdims=False)
        pairs = [(i, (i + shift) % n_hi) for i in range(n_hi)]
        total = total + lax.ppermute(outgoing, "z_hi", pairs).astype(jnp.float32)
    return total


def solution(mesh):
    n_fsdp, n_tensor = mesh.devices.shape
    n_x = 4 if n_fsdp % 4 == 0 else n_fsdp
    parts = mesh.devices.reshape(n_fsdp // n_x, n_x, 2, n_tensor // 4, 2)
    fine = Mesh(parts, ("z_hi", "x", "z_lo", "y", "core"))
    return jax.shard_map(
        body,
        mesh=fine,
        in_specs=(P(FSDP, None), P(FSDP, None, TENSOR), P(FSDP, None, TENSOR), P()),
        out_specs=P(FSDP, None, TENSOR),
        check_vma=False,
    )
```
